128 devices in a mesh: freq: 8 (over y, core), outp: 8 (over x, z_lo), inp: 2 (over z_hi).
Axes of the slice: x: 4, y: 4, z: 4 (z_hi: 2, z_lo: 2; z = z_hi * 2 + z_lo), core: 2. Of those that a mesh axis runs over, the one named last changes fastest.
Arguments:
- measured: float32 [2, 8, 2048, 2048], P(None, 'freq', 'outp', 'inp'), may hold values from -6 to 6
- left_factor: bfloat16 [2048, 4096], P('outp', 'freq'), may hold values from -0.75 to 0.75
- right_factor: bfloat16 [4096, 2048], P('freq', 'inp'), may hold values from -0.75 to 0.75
- pole_rates: float32 [512], replicated, may hold values from 0.5 to 8
- sample_freqs: float32 [8], P('freq'), may hold values from 0 to 8
Outputs:
- grad_left: float32 [2048, 4096], P('outp', ('freq', 'inp'))
- grad_right: float32 [4096, 2048], P(('freq', 'outp'), 'inp')
The draws below stay inside these ranges and needn't reach their ends.
All inputs are finite; a program needn't handle non-finite values.
Results may differ from the reference program's by a relative error of at most 0.0003.
Values may be sent and summed in bfloat16 or wider, within the bound.
No kernel may reach another device: no remote copies, remote signals or barrier semaphores. Data moves between devices by JAX's collectives and lax.ppermute only.
A program may use at most 128 MiB of HBM per device.

```python
import math
import jax
import jax.numpy as jnp
from jax import lax

PORTS = 2048
POLES = 512
RANK = 8
RANKS = 4096
FREQS = 8


def block_scale(own_key, extent, pieces, least, high):
    factor_of, own = 1.0, jax.random.fold_in(own_key, 6)
    for axis_at, blocks in pieces:
        draws = jnp.exp(jax.random.uniform(jax.random.fold_in(own, axis_at), (blocks,), jnp.float32, least / len(pieces), high / len(pieces)))
        factor_of = factor_of * jnp.repeat(draws, extent[axis_at] // blocks).reshape([-1 if axis == axis_at else 1 for axis in range(len(extent))])
    return factor_of


def gaussian(rng, extent, spread, bound, shards=(), kind=jnp.bfloat16):
    values = spread * jax.random.normal(rng, extent, jnp.float32)
    if shards:
        values = values * block_scale(rng, extent, shards, -0.22, 0.18)
    return jnp.clip(values, -bound, bound).astype(kind)


def setup_inputs(seed: int = 0) -> dict:
    splits = jax.random.split(jax.random.key(seed), 6)
    measured = gaussian(splits[0], (2, FREQS, PORTS, PORTS), 1.0, 6.0, ((1, 8), (2, 8), (3, 2)), jnp.float32)
    left_factor = gaussian(splits[1], (PORTS, RANKS), 0.125, 0.75, ((0, 8), (1, 8)))
    right_factor = gaussian(splits[2], (RANKS, PORTS), 0.125, 0.75, ((0, 8), (1, 2)))
    pole_rates = jnp.clip(jnp.exp(jax.random.uniform(splits[3], (POLES,), jnp.float32, math.log(0.5), math.log(8.0))), 0.5, 8.0)
    sample_freqs = jnp.clip(8.0 * jax.random.uniform(splits[4], (FREQS,), jnp.float32) ** block_scale(splits[4], (FREQS,), ((0, 8),), -0.2, 0.2), 0.0, 8.0)
    return dict(measured=measured, left_factor=left_factor, right_factor=right_factor, pole_rates=pole_rates, sample_freqs=sample_freqs)


def responses(omega, pole_rates):
    denominator = pole_rates * pole_rates + omega * omega
    real_resp = jnp.repeat(pole_rates / denominator, RANK)
    imag_resp = jnp.repeat(-omega / denominator, RANK)
    return (real_resp, imag_resp)

def reference(measured, left_factor, right_factor, pole_rates, sample_freqs):
    left_wide = left_factor.astype(jnp.float32)
    right_wide = right_factor.astype(jnp.float32)
    highest = lax.Precision.HIGHEST

    def one_sample(totals, sample):
        left_acc, right_acc = totals
        real_resp, imag_resp = responses(sample_freqs[sample], pole_rates)
        scaled = jnp.concatenate([left_wide * real_resp[None, :], left_wide * imag_resp[None, :]], 0)
        fitted = jnp.dot(scaled, right_wide, precision=highest, preferred_element_type=jnp.float32)
        observed = lax.dynamic_index_in_dim(measured, sample, 1, keepdims=False).reshape(2 * PORTS, PORTS)
        misfit = fitted - observed
        backward = lax.dot_general(misfit, right_wide, (((1,), (1,)), ((), ())), precision=highest, preferred_element_type=jnp.float32)
        left_acc = left_acc + backward[:PORTS] * real_resp[None, :] + backward[PORTS:] * imag_resp[None, :]
        right_acc = right_acc + lax.dot_general(scaled, misfit, (((0,), (0,)), ((), ())), precision=highest, preferred_element_type=jnp.float32)
        return ((left_acc, right_acc), None)
    start_totals = (jnp.zeros((PORTS, RANKS), jnp.float32), jnp.zeros((RANKS, PORTS), jnp.float32))
    totals, _ = lax.scan(one_sample, start_totals, jnp.arange(FREQS, dtype=jnp.int32))
    grad_scale = float(RANKS) ** 0.25 / math.sqrt(float(FREQS * PORTS))
    return (totals[0] * grad_scale, totals[1] * grad_scale)
```

```python
import math

import jax
import jax.numpy as jnp
from jax import lax
from jax.sharding import PartitionSpec as P

PORTS = 2048
RANK = 8
RANKS = 4096


def shards(measured, left_factor, right_factor, pole_rates, sample_freqs):
    highest = lax.Precision.HIGHEST
    n_freq = lax.axis_size("freq")
    n_outp = lax.axis_size("outp")
    observed = lax.all_to_all(measured, "freq", 3, 1, tiled=True)
    right_cols = lax.all_to_all(right_factor, "freq", 1, 0, tiled=True)
    left_whole = lax.all_gather(left_factor, "freq", axis=1, tiled=True)
    omegas = lax.all_gather(sample_freqs, "freq", axis=0, tiled=True)
    total_samples = omegas.shape[0]
    grad_scale = float(RANKS) ** 0.25 / math.sqrt(float(total_samples * PORTS))
    left_wide = left_whole.astype(jnp.float32)
    right_wide = right_cols.astype(jnp.float32)
    denominator = pole_rates[None, :] * pole_rates[None, :] + omegas[:, None] * omegas[:, None]
    real_resp = jnp.repeat(pole_rates[None, :] / denominator, RANK, axis=1)
    imag_resp = jnp.repeat(-omegas[:, None] / denominator, RANK, axis=1)
    resp = jnp.stack([real_resp, imag_resp], 0)
    scaled_right = resp[:, :, :, None] * right_wide[None, None]
    fitted = jnp.einsum("rk,pfkj->pfrj", left_wide, scaled_right, precision=highest,
                        preferred_element_type=jnp.float32)
    misfit = fitted - observed
    grad_left = jnp.einsum("pfrj,pfkj->rk", misfit, scaled_right, precision=highest,
                           preferred_element_type=jnp.float32)
    scaled_left = resp[:, :, None, :] * left_wide[None, None]
    grad_right = jnp.einsum("pfrk,pfrj->kj", scaled_left, misfit, precision=highest,
                            preferred_element_type=jnp.float32)
    grad_left = lax.psum_scatter(grad_left * grad_scale, ("freq", "inp"), scatter_dimension=1, tiled=True)
    k_rows, j_cols = grad_right.shape
    block = k_rows // (n_freq * n_outp)
    grad_right = (grad_right * grad_scale).reshape(n_freq, n_outp, block, j_cols)
    grad_right = grad_right.transpose(1, 0, 2, 3).reshape(n_outp * n_freq * block, j_cols)
    grad_right = lax.psum_scatter(grad_right, "outp", scatter_dimension=0, tiled=True)
    grad_right = grad_right.reshape(n_freq, block, j_cols)
    grad_right = lax.all_to_all(grad_right, "freq", 0, 2, tiled=True)
    grad_right = grad_right.reshape(block, n_freq * j_cols)
    return (grad_left, grad_right)


def solution(mesh):
    return jax.shard_map(
        shards,
        mesh=mesh,
        in_specs=(
            P(None, "freq", "outp", "inp"),
            P("outp", "freq"),
            P("freq", "inp"),
            P(),
            P("freq"),
        ),
        out_specs=(P("outp", ("freq", "inp")), P(("freq", "outp"), "inp")),
        check_vma=False,
    )
```

```python
import math

import jax
import jax.numpy as jnp
from jax import lax
from jax.sharding import PartitionSpec as P

PORTS = 2048
RANK = 8
RANKS = 4096


def shards(measured, left_factor, right_factor, pole_rates, sample_freqs):
    highest = lax.Precision.HIGH
    n_freq = lax.axis_size("freq")
    n_outp = lax.axis_size("outp")
    two, _, out_rows, in_cols = measured.shape
    tagged = jnp.concatenate(
        [measured, jnp.broadcast_to(sample_freqs[0], (two, 1, 8, in_cols))], axis=2)
    tagged = lax.all_to_all(tagged, "freq", 3, 1, tiled=True)
    observed = tagged[:, :, :out_rows, :]
    omegas = tagged[0, :, out_rows, 0]
    right_cols = lax.all_to_all(right_factor, "freq", 1, 0, tiled=True)
    left_whole = lax.all_gather(left_factor, "freq", axis=1, tiled=True)
    total_samples = omegas.shape[0]
    grad_scale = float(RANKS) ** 0.25 / math.sqrt(float(total_samples * PORTS))
    left_wide = left_whole.astype(jnp.float32)
    right_wide = right_cols.astype(jnp.float32)
    denominator = pole_rates[None, :] * pole_rates[None, :] + omegas[:, None] * omegas[:, None]
    real_resp = jnp.repeat(pole_rates[None, :] / denominator, RANK, axis=1)
    imag_resp = jnp.repeat(-omegas[:, None] / denominator, RANK, axis=1)
    resp = jnp.stack([real_resp, imag_resp], 0)
    scaled_right = resp[:, :, :, None] * right_wide[None, None]
    fitted = jnp.einsum("rk,pfkj->pfrj", left_wide, scaled_right, precision=highest,
                        preferred_element_type=jnp.float32)
    misfit = fitted - observed
    grad_left = jnp.einsum("pfrj,pfkj->rk", misfit, scaled_right, precision=highest,
                           preferred_element_type=jnp.float32)
    scaled_left = resp[:, :, None, :] * left_wide[None, None]
    grad_right = jnp.einsum("pfrk,pfrj->kj", scaled_left, misfit, precision=highest,
                            preferred_element_type=jnp.float32)
    grad_left = lax.psum_scatter(grad_left * grad_scale, ("freq", "inp"), scatter_dimension=1, tiled=True)
    k_rows, j_cols = grad_right.shape
    block = k_rows // (n_freq * n_outp)
    grad_right = (grad_right * grad_scale).reshape(n_freq, n_outp, block, j_cols)
    grad_right = grad_right.transpose(1, 0, 2, 3).reshape(n_outp * n_freq * block, j_cols)
    grad_right = lax.psum_scatter(grad_right, "outp", scatter_dimension=0, tiled=True)
    grad_right = grad_right.reshape(n_freq, block, j_cols)
    grad_right = lax.all_to_all(grad_right, "freq", 0, 2, tiled=True)
    grad_right = grad_right.reshape(block, n_freq * j_cols)
    return (grad_left, grad_right)


def solution(mesh):
    return jax.shard_map(
        shards,
        mesh=mesh,
        in_specs=(
            P(None, "freq", "outp", "inp"),
            P("outp", "freq"),
            P("freq", "inp"),
            P(),
            P("freq"),
        ),
        out_specs=(P("outp", ("freq", "inp")), P(("freq", "outp"), "inp")),
        check_vma=False,
    )
```

```python
import math

import jax
import jax.numpy as jnp
from jax import lax
from jax.sharding import PartitionSpec as P

PORTS = 2048
RANK = 8
RANKS = 4096


def shards(measured, left_factor, right_factor, pole_rates, sample_freqs):
    precision = lax.Precision.HIGH
    n_freq = lax.axis_size("freq")
    n_outp = lax.axis_size("outp")
    two, _, out_rows, in_cols = measured.shape
    half = out_rows // 2
    first = jnp.concatenate(
        [measured[:, :, :half], jnp.broadcast_to(sample_freqs[0], (two, 1, 8, in_cols))], axis=2)
    first = lax.all_to_all(first, "freq", 3, 1, tiled=True)
    omegas = first[0, :, half, 0]
    observed = (first[:, :, :half], lax.all_to_all(measured[:, :, half:], "freq", 3, 1, tiled=True))
    right_cols = lax.all_to_all(right_factor, "freq", 1, 0, tiled=True)
    left_whole = lax.all_gather(left_factor, "freq", axis=1, tiled=True)
    total_samples = omegas.shape[0]
    grad_scale = float(RANKS) ** 0.25 / math.sqrt(float(total_samples * PORTS))
    right_wide = right_cols.astype(jnp.float32)
    denominator = pole_rates[None, :] * pole_rates[None, :] + omegas[:, None] * omegas[:, None]
    real_resp = jnp.repeat(pole_rates[None, :] / denominator, RANK, axis=1)
    imag_resp = jnp.repeat(-omegas[:, None] / denominator, RANK, axis=1)
    resp = jnp.stack([real_resp, imag_resp], 0)
    scaled_right = resp[:, :, :, None] * right_wide[None, None]
    grad_left = []
    grad_right = None
    for h in range(2):
        left_wide = left_whole[h * half:(h + 1) * half].astype(jnp.float32)
        fitted = jnp.einsum("rk,pfkj->pfrj", left_wide, scaled_right, precision=precision,
                            preferred_element_type=jnp.float32)
        misfit = fitted - observed[h]
        part = jnp.einsum("pfrj,pfkj->rk", misfit, scaled_right, precision=precision,
                          preferred_element_type=jnp.float32)
        grad_left.append(lax.psum_scatter(part * grad_scale, ("freq", "inp"),
                                          scatter_dimension=1, tiled=True))
        scaled_left = resp[:, :, None, :] * left_wide[None, None]
        term = jnp.einsum("pfrk,pfrj->kj", scaled_left, misfit, precision=precision,
                          preferred_element_type=jnp.float32)
        grad_right = term if grad_right is None else grad_right + term
    grad_left = jnp.concatenate(grad_left, 0)
    k_rows, j_cols = grad_right.shape
    block = k_rows // (n_freq * n_outp)
    grad_right = (grad_right * grad_scale).reshape(n_freq, n_outp, block, j_cols)
    grad_right = lax.all_to_all(grad_right, "outp", 1, 1, tiled=True)
    grad_right = jnp.sum(grad_right, axis=1)
    grad_right = lax.all_to_all(grad_right, "freq", 0, 2, tiled=True)
    grad_right = grad_right.reshape(block, n_freq * j_cols)
    return (grad_left, grad_right)


def solution(mesh):
    return jax.shard_map(
        shards,
        mesh=mesh,
        in_specs=(
            P(None, "freq", "outp", "inp"),
            P("outp", "freq"),
            P("freq", "inp"),
            P(),
            P("freq"),
        ),
        out_specs=(P("outp", ("freq", "inp")), P(("freq", "outp"), "inp")),
        check_vma=False,
    )
```

```python
import math

import jax
import jax.numpy as jnp
from jax import lax
from jax.sharding import PartitionSpec as P

PORTS = 2048
RANK = 8
RANKS = 4096


def shards(measured, left_factor, right_factor, pole_rates, sample_freqs):
    highest = lax.Precision.HIGH
    n_freq = lax.axis_size("freq")
    n_outp = lax.axis_size("outp")
    two, _, out_rows, in_cols = measured.shape
    tagged = jnp.concatenate(
        [measured, jnp.broadcast_to(sample_freqs[0], (two, 1, 8, in_cols))], axis=2)
    tagged = lax.all_to_all(tagged, "freq", 3, 1, tiled=True)
    observed = tagged[:, :, :out_rows, :]
    omegas = tagged[0, :, out_rows, 0]
    right_cols = lax.all_to_all(right_factor, "freq", 1, 0, tiled=True)
    left_whole = lax.all_gather(left_factor, "freq", axis=1, tiled=True)
    total_samples = omegas.shape[0]
    grad_scale = float(RANKS) ** 0.25 / math.sqrt(float(total_samples * PORTS))
    left_wide = left_whole.astype(jnp.float32)
    right_wide = right_cols.astype(jnp.float32)
    denominator = pole_rates[None, :] * pole_rates[None, :] + omegas[:, None] * omegas[:, None]
    real_resp = jnp.repeat(pole_rates[None, :] / denominator, RANK, axis=1)
    imag_resp = jnp.repeat(-omegas[:, None] / denominator, RANK, axis=1)
    resp = jnp.stack([real_resp, imag_resp], 0)
    scaled_right = resp[:, :, :, None] * right_wide[None, None]
    fitted = jnp.einsum("rk,pfkj->pfrj", left_wide, scaled_right, precision=highest,
                        preferred_element_type=jnp.float32)
    misfit = fitted - observed
    grad_left = jnp.einsum("pfrj,pfkj->rk", misfit, scaled_right, precision=highest,
                           preferred_element_type=jnp.float32)
    grad_left = lax.psum_scatter(grad_left * grad_scale, ("freq", "inp"), scatter_dimension=1, tiled=True)
    scaled_left = resp[:, :, None, :] * left_wide[None, None]
    grad_right = jnp.einsum("pfrk,pfrj->kj", scaled_left, misfit, precision=highest,
                            preferred_element_type=jnp.float32)
    k_rows, j_cols = grad_right.shape
    block = k_rows // (n_freq * n_outp)
    grad_right = (grad_right * grad_scale).reshape(n_freq, n_outp, block, j_cols)
    grad_right = lax.all_to_all(grad_right, "outp", 1, 1, tiled=True)
    grad_right = jnp.sum(grad_right, axis=1)
    grad_right = lax.all_to_all(grad_right, "freq", 0, 2, tiled=True)
    grad_right = grad_right.reshape(block, n_freq * j_cols)
    return (grad_left, grad_right)


def solution(mesh):
    return jax.shard_map(
        shards,
        mesh=mesh,
        in_specs=(
            P(None, "freq", "outp", "inp"),
            P("outp", "freq"),
            P("freq", "inp"),
            P(),
            P("freq"),
        ),
        out_specs=(P("outp", ("freq", "inp")), P(("freq", "outp"), "inp")),
        check_vma=False,
    )
```

```python
import math

import jax
import jax.numpy as jnp
from jax import lax
from jax.sharding import PartitionSpec as P

PORTS = 2048
RANK = 8
RANKS = 4096


def shards(measured, left_factor, right_factor, pole_rates, sample_freqs):
    highest = lax.Precision.HIGH
    n_freq = lax.axis_size("freq")
    n_outp = lax.axis_size("outp")
    two, _, out_rows, in_cols = measured.shape
    k_block, _ = right_factor.shape
    chunks = right_factor.reshape(k_block, n_freq, in_cols // n_freq).transpose(1, 0, 2)
    chunks = lax.all_to_all(chunks, "freq", 0, 0, tiled=True)
    right_cols = chunks.reshape(n_freq * k_block, in_cols // n_freq)
    tagged = jnp.concatenate(
        [measured, jnp.broadcast_to(sample_freqs[0], (two, 1, 8, in_cols))], axis=2)
    tagged = lax.all_to_all(tagged, "freq", 3, 1, tiled=True)
    observed = tagged[:, :, :out_rows, :]
    omegas = tagged[0, :, out_rows, 0]
    left_whole = lax.all_gather(left_factor, "freq", axis=1, tiled=True)
    total_samples = omegas.shape[0]
    grad_scale = float(RANKS) ** 0.25 / math.sqrt(float(total_samples * PORTS))
    left_wide = left_whole.astype(jnp.float32)
    right_wide = right_cols.astype(jnp.float32)
    denominator = pole_rates[None, :] * pole_rates[None, :] + omegas[:, None] * omegas[:, None]
    real_resp = jnp.repeat(pole_rates[None, :] / denominator, RANK, axis=1)
    imag_resp = jnp.repeat(-omegas[:, None] / denominator, RANK, axis=1)
    resp = jnp.stack([real_resp, imag_resp], 0)
    scaled_right = resp[:, :, :, None] * right_wide[None, None]
    fitted = jnp.einsum("rk,pfkj->pfrj", left_wide, scaled_right, precision=highest,
                        preferred_element_type=jnp.float32)
    misfit = fitted - observed
    grad_left = jnp.einsum("pfrj,pfkj->rk", misfit, scaled_right, precision=highest,
                           preferred_element_type=jnp.float32)
    grad_left = lax.psum_scatter(grad_left * grad_scale, ("freq", "inp"), scatter_dimension=1, tiled=True)
    scaled_left = resp[:, :, None, :] * left_wide[None, None]
    grad_right = jnp.einsum("pfrk,pfrj->kj", scaled_left, misfit, precision=highest,
                            preferred_element_type=jnp.float32)
    k_rows, j_cols = grad_right.shape
    block = k_rows // (n_freq * n_outp)
    grad_right = (grad_right * grad_scale).reshape(n_freq, n_outp, block, j_cols)
    grad_right = lax.all_to_all(grad_right, "outp", 1, 1, tiled=True)
    grad_right = jnp.sum(grad_right, axis=1)
    grad_right = lax.all_to_all(grad_right, "freq", 0, 2, tiled=True)
    grad_right = grad_right.reshape(block, n_freq * j_cols)
    return (grad_left, grad_right)


def solution(mesh):
    return jax.shard_map(
        shards,
        mesh=mesh,
        in_specs=(
            P(None, "freq", "outp", "inp"),
            P("outp", "freq"),
            P("freq", "inp"),
            P(),
            P("freq"),
        ),
        out_specs=(P("outp", ("freq", "inp")), P(("freq", "outp"), "inp")),
        check_vma=False,
    )
```

```python
import math

import jax
import jax.numpy as jnp
from jax import lax
from jax.sharding import PartitionSpec as P

PORTS = 2048
RANK = 8
RANKS = 4096


def shards(measured, left_factor, right_factor, pole_rates, sample_freqs):
    highest = lax.Precision.HIGH
    n_freq = lax.axis_size("freq")
    n_outp = lax.axis_size("outp")
    two, _, out_rows, in_cols = measured.shape
    k_block = right_factor.shape[0]
    tagged = jnp.concatenate(
        [measured, jnp.broadcast_to(sample_freqs[0], (two, 1, 8, in_cols))], axis=2)
    tag_rows = two * (out_rows + 8)
    packed = jnp.concatenate(
        [tagged.reshape(tag_rows, in_cols), right_factor.astype(jnp.float32)], axis=0)
    packed = lax.all_to_all(packed, "freq", 1, 0, tiled=True)
    packed = packed.reshape(n_freq, tag_rows + k_block, in_cols // n_freq)
    tagged = packed[:, :tag_rows].reshape(n_freq, two, out_rows + 8, in_cols // n_freq)
    observed = tagged[:, :, :out_rows].transpose(1, 0, 2, 3)
    omegas = tagged[:, 0, out_rows, 0]
    right_wide = packed[:, tag_rows:].reshape(n_freq * k_block, in_cols // n_freq)
    left_whole = lax.all_gather(left_factor, "freq", axis=1, tiled=True)
    total_samples = omegas.shape[0]
    grad_scale = float(RANKS) ** 0.25 / math.sqrt(float(total_samples * PORTS))
    left_wide = left_whole.astype(jnp.float32)
    denominator = pole_rates[None, :] * pole_rates[None, :] + omegas[:, None] * omegas[:, None]
    real_resp = jnp.repeat(pole_rates[None, :] / denominator, RANK, axis=1)
    imag_resp = jnp.repeat(-omegas[:, None] / denominator, RANK, axis=1)
    resp = jnp.stack([real_resp, imag_resp], 0)
    scaled_right = resp[:, :, :, None] * right_wide[None, None]
    fitted = jnp.einsum("rk,pfkj->pfrj", left_wide, scaled_right, precision=highest,
                        preferred_element_type=jnp.float32)
    misfit = fitted - observed
    grad_left = jnp.einsum("pfrj,pfkj->rk", misfit, scaled_right, precision=highest,
                           preferred_element_type=jnp.float32)
    grad_left = lax.psum_scatter(grad_left * grad_scale, ("freq", "inp"), scatter_dimension=1, tiled=True)
    scaled_left = resp[:, :, None, :] * left_wide[None, None]
    grad_right = jnp.einsum("pfrk,pfrj->kj", scaled_left, misfit, precision=highest,
                            preferred_element_type=jnp.float32)
    k_rows, j_cols = grad_right.shape
    block = k_rows // (n_freq * n_outp)
    grad_right = (grad_right * grad_scale).reshape(n_freq, n_outp, block, j_cols)
    grad_right = lax.all_to_all(grad_right, "outp", 1, 1, tiled=True)
    grad_right = jnp.sum(grad_right, axis=1)
    grad_right = lax.all_to_all(grad_right, "freq", 0, 2, tiled=True)
    grad_right = grad_right.reshape(block, n_freq * j_cols)
    return (grad_left, grad_right)


def solution(mesh):
    return jax.shard_map(
        shards,
        mesh=mesh,
        in_specs=(
            P(None, "freq", "outp", "inp"),
            P("outp", "freq"),
            P("freq", "inp"),
            P(),
            P("freq"),
        ),
        out_specs=(P("outp", ("freq", "inp")), P(("freq", "outp"), "inp")),
        check_vma=False,
    )
```

```python
import math

import jax
import jax.numpy as jnp
from jax import lax
from jax.sharding import PartitionSpec as P

PORTS = 2048
RANK = 8
RANKS = 4096


def shards(measured, left_factor, right_factor, pole_rates, sample_freqs):
    highest = lax.Precision.HIGH
    n_freq = lax.axis_size("freq")
    n_outp = lax.axis_size("outp")
    two, _, out_rows, in_cols = measured.shape
    tagged = jnp.concatenate(
        [measured, jnp.broadcast_to(sample_freqs[0], (two, 1, 8, in_cols))], axis=2)
    tagged = lax.all_to_all(tagged, "freq", 3, 1, tiled=True)
    observed = tagged[:, :, :out_rows, :]
    omegas = tagged[0, :, out_rows, 0]
    right_cols = lax.all_to_all(right_factor, "freq", 1, 0, tiled=True)
    left_whole = lax.all_gather(left_factor, "freq", axis=1, tiled=True)
    total_samples = omegas.shape[0]
    grad_scale = float(RANKS) ** 0.25 / math.sqrt(float(total_samples * PORTS))
    left_wide = left_whole.astype(jnp.float32)
    right_wide = right_cols.astype(jnp.float32)
    denominator = pole_rates[None, :] * pole_rates[None, :] + omegas[:, None] * omegas[:, None]
    real_resp = jnp.repeat(pole_rates[None, :] / denominator, RANK, axis=1)
    imag_resp = jnp.repeat(-omegas[:, None] / denominator, RANK, axis=1)
    resp = jnp.stack([real_resp, imag_resp], 0)
    scaled_right = resp[:, :, :, None] * right_wide[None, None]
    fitted = jnp.einsum("rk,pfkj->pfrj", left_wide, scaled_right, precision=highest,
                        preferred_element_type=jnp.float32)
    misfit = fitted - observed
    n_dest = n_freq * lax.axis_size("inp")
    k_all = scaled_right.shape[2]
    sub = k_all // n_dest // 2
    pieces = []
    for c in range(2):
        cols = scaled_right.reshape(2, n_freq, n_dest, 2, sub, -1)[:, :, :, c]
        cols = cols.reshape(2, n_freq, n_dest * sub, -1)
        piece = jnp.einsum("pfrj,pfkj->rk", misfit, cols, precision=highest,
                           preferred_element_type=jnp.float32)
        pieces.append(lax.psum_scatter(piece * grad_scale, ("freq", "inp"),
                                       scatter_dimension=1, tiled=True))
    grad_left = jnp.concatenate(pieces, axis=1)
    scaled_left = resp[:, :, None, :] * left_wide[None, None]
    grad_right = jnp.einsum("pfrk,pfrj->kj", scaled_left, misfit, precision=highest,
                            preferred_element_type=jnp.float32)
    k_rows, j_cols = grad_right.shape
    block = k_rows // (n_freq * n_outp)
    grad_right = (grad_right * grad_scale).reshape(n_freq, n_outp, block, j_cols)
    grad_right = lax.all_to_all(grad_right, "outp", 1, 1, tiled=True)
    grad_right = jnp.sum(grad_right, axis=1)
    grad_right = lax.all_to_all(grad_right, "freq", 0, 2, tiled=True)
    grad_right = grad_right.reshape(block, n_freq * j_cols)
    return (grad_left, grad_right)


def solution(mesh):
    return jax.shard_map(
        shards,
        mesh=mesh,
        in_specs=(
            P(None, "freq", "outp", "inp"),
            P("outp", "freq"),
            P("freq", "inp"),
            P(),
            P("freq"),
        ),
        out_specs=(P("outp", ("freq", "inp")), P(("freq", "outp"), "inp")),
        check_vma=False,
    )
```

```python
import math

import jax
import jax.numpy as jnp
from jax import lax
from jax.sharding import PartitionSpec as P


PORTS = 2048
RANK = 8
RANKS = 4096


def shards(measured, left_factor, right_factor, pole_rates, sample_freqs):
    highest = lax.Precision.HIGH
    n_freq = lax.axis_size("freq")
    n_outp = lax.axis_size("outp")
    _, _, _, in_cols = measured.shape
    k_block = right_factor.shape[0]
    j_cols = in_cols // n_freq
    omega = sample_freqs[0]
    omega_hi = omega.astype(jnp.bfloat16)
    rest = omega - omega_hi.astype(jnp.float32)
    omega_mid = rest.astype(jnp.bfloat16)
    omega_lo = (rest - omega_mid.astype(jnp.float32)).astype(jnp.bfloat16)
    terms = jnp.zeros((8,), jnp.bfloat16).at[0].set(omega_hi).at[1].set(omega_mid).at[2].set(omega_lo)
    chunks = right_factor.reshape(k_block, n_freq, j_cols).transpose(1, 0, 2)
    chunks = jnp.concatenate(
        [chunks, jnp.broadcast_to(terms[None, :, None], (n_freq, 8, j_cols))], axis=1)
    chunks = lax.all_to_all(chunks, "freq", 0, 0, tiled=True)
    parts = chunks[:, k_block:k_block + 3, 0].astype(jnp.float32)
    omegas = (parts[:, 0] + parts[:, 1]) + parts[:, 2]
    right_cols = chunks[:, :k_block].reshape(n_freq * k_block, j_cols)
    observed = lax.all_to_all(measured, "freq", 3, 1, tiled=True)
    left_whole = lax.all_gather(left_factor, "freq", axis=1, tiled=True)
    total_samples = omegas.shape[0]
    grad_scale = float(RANKS) ** 0.25 / math.sqrt(float(total_samples * PORTS))
    left_wide = left_whole.astype(jnp.float32)
    right_wide = right_cols.astype(jnp.float32)
    denominator = pole_rates[None, :] * pole_rates[None, :] + omegas[:, None] * omegas[:, None]
    real_resp = jnp.repeat(pole_rates[None, :] / denominator, RANK, axis=1)
    imag_resp = jnp.repeat(-omegas[:, None] / denominator, RANK, axis=1)
    resp = jnp.stack([real_resp, imag_resp], 0)
    scaled_right = resp[:, :, :, None] * right_wide[None, None]
    fitted = jnp.einsum("rk,pfkj->pfrj", left_wide, scaled_right, precision=highest,
                        preferred_element_type=jnp.float32)
    fitted = lax.optimization_barrier(fitted)
    misfit = fitted - observed
    grad_left = jnp.einsum("pfrj,pfkj->rk", misfit, scaled_right, precision=highest,
                           preferred_element_type=jnp.float32)
    grad_left = lax.psum_scatter(grad_left * grad_scale, "freq", scatter_dimension=1, tiled=True)
    grad_left = lax.psum_scatter(grad_left, "inp", scatter_dimension=1, tiled=True)
    scaled_left = resp[:, :, None, :] * left_wide[None, None]
    grad_right = jnp.einsum("pfrk,pfrj->kj", scaled_left, misfit, precision=highest,
                            preferred_element_type=jnp.float32)
    k_rows, j_cols = grad_right.shape
    block = k_rows // (n_freq * n_outp)
    grad_right = (grad_right * grad_scale).reshape(n_freq, n_outp, block, j_cols)
    grad_right = lax.all_to_all(grad_right, "outp", 1, 1, tiled=True)
    grad_right = jnp.sum(grad_right, axis=1)
    grad_right = lax.all_to_all(grad_right, "freq", 0, 2, tiled=True)
    grad_right = grad_right.reshape(block, n_freq * j_cols)
    return (grad_left, grad_right)


def solution(mesh):
    return jax.shard_map(
        shards,
        mesh=mesh,
        in_specs=(
            P(None, "freq", "outp", "inp"),
            P("outp", "freq"),
            P("freq", "inp"),
            P(),
            P("freq"),
        ),
        out_specs=(P("outp", ("freq", "inp")), P(("freq", "outp"), "inp")),
        check_vma=False,
    )
```

```python
import math

import jax
import jax.numpy as jnp
from jax import lax
from jax.sharding import PartitionSpec as P


PORTS = 2048
RANK = 8
RANKS = 4096


def shards(measured, left_factor, right_factor, pole_rates, sample_freqs):
    highest = lax.Precision.HIGH
    n_freq = lax.axis_size("freq")
    n_outp = lax.axis_size("outp")
    _, _, _, in_cols = measured.shape
    k_block = right_factor.shape[0]
    j_cols = in_cols // n_freq
    omega = sample_freqs[0]
    omega_hi = omega.astype(jnp.bfloat16)
    rest = omega - omega_hi.astype(jnp.float32)
    omega_mid = rest.astype(jnp.bfloat16)
    omega_lo = (rest - omega_mid.astype(jnp.float32)).astype(jnp.bfloat16)
    terms = jnp.zeros((8,), jnp.bfloat16).at[0].set(omega_hi).at[1].set(omega_mid).at[2].set(omega_lo)
    chunks = right_factor.reshape(k_block, n_freq, j_cols).transpose(1, 0, 2)
    chunks = jnp.concatenate(
        [chunks, jnp.broadcast_to(terms[None, :, None], (n_freq, 8, j_cols))], axis=1)
    chunks = lax.all_to_all(chunks, "freq", 0, 0, tiled=True)
    parts = chunks[:, k_block:k_block + 3, 0].astype(jnp.float32)
    omegas = (parts[:, 0] + parts[:, 1]) + parts[:, 2]
    right_cols = chunks[:, :k_block].reshape(n_freq * k_block, j_cols)
    observed = lax.all_to_all(measured, "freq", 3, 1, tiled=True)
    left_whole = lax.all_gather(left_factor, "freq", axis=1, tiled=True)
    total_samples = omegas.shape[0]
    grad_scale = float(RANKS) ** 0.25 / math.sqrt(float(total_samples * PORTS))
    left_wide = left_whole.astype(jnp.float32)
    right_wide = right_cols.astype(jnp.float32)
    denominator = pole_rates[None, :] * pole_rates[None, :] + omegas[:, None] * omegas[:, None]
    real_resp = jnp.repeat(pole_rates[None, :] / denominator, RANK, axis=1)
    imag_resp = jnp.repeat(-omegas[:, None] / denominator, RANK, axis=1)
    resp = jnp.stack([real_resp, imag_resp], 0)
    scaled_right = resp[:, :, :, None] * right_wide[None, None]
    fitted = jnp.einsum("rk,pfkj->pfrj", left_wide, scaled_right, precision=highest,
                        preferred_element_type=jnp.float32)
    fitted = lax.optimization_barrier(fitted)
    misfit = fitted - observed
    grad_left = jnp.einsum("pfrj,pfkj->rk", misfit, scaled_right, precision=highest,
                           preferred_element_type=jnp.float32)
    grad_left = lax.psum_scatter(grad_left * grad_scale, "freq", scatter_dimension=1, tiled=True)
    grad_left = lax.psum_scatter(grad_left, "inp", scatter_dimension=1, tiled=True)
    scaled_left = resp[:, :, None, :] * left_wide[None, None]
    grad_right = jnp.einsum("pfrk,pfrj->kj", scaled_left, misfit, precision=highest,
                            preferred_element_type=jnp.float32)
    k_rows, j_cols = grad_right.shape
    block = k_rows // (n_freq * n_outp)
    grad_right = (grad_right * grad_scale).reshape(n_freq, n_outp, block, j_cols)
    half_block = block // 2
    by_exchange = lax.all_to_all(grad_right[:, :, :half_block], "outp", 1, 1, tiled=True)
    by_exchange = jnp.sum(by_exchange, axis=1)
    by_queue = grad_right[:, :, half_block:].transpose(1, 0, 2, 3)
    by_queue = by_queue.reshape(n_outp * n_freq * (block - half_block), j_cols)
    by_queue = lax.psum_scatter(by_queue, "outp", scatter_dimension=0, tiled=True)
    by_queue = by_queue.reshape(n_freq, block - half_block, j_cols)
    grad_right = jnp.concatenate([by_exchange, by_queue], axis=1)
    grad_right = lax.all_to_all(grad_right, "freq", 0, 2, tiled=True)
    grad_right = grad_right.reshape(block, n_freq * j_cols)
    return (grad_left, grad_right)


def solution(mesh):
    return jax.shard_map(
        shards,
        mesh=mesh,
        in_specs=(
            P(None, "freq", "outp", "inp"),
            P("outp", "freq"),
            P("freq", "inp"),
            P(),
            P("freq"),
        ),
        out_specs=(P("outp", ("freq", "inp")), P(("freq", "outp"), "inp")),
        check_vma=False,
    )
```

```python
import math

import jax
import jax.numpy as jnp
from jax import lax
from jax.sharding import PartitionSpec as P


PORTS = 2048
RANK = 8
RANKS = 4096


def shards(measured, left_factor, right_factor, pole_rates, sample_freqs):
    highest = lax.Precision.HIGH
    n_freq = lax.axis_size("freq")
    n_outp = lax.axis_size("outp")
    _, _, _, in_cols = measured.shape
    k_block = right_factor.shape[0]
    j_cols = in_cols // n_freq
    omega = sample_freqs[0]
    omega_hi = omega.astype(jnp.bfloat16)
    rest = omega - omega_hi.astype(jnp.float32)
    omega_mid = rest.astype(jnp.bfloat16)
    omega_lo = (rest - omega_mid.astype(jnp.float32)).astype(jnp.bfloat16)
    terms = jnp.zeros((8,), jnp.bfloat16).at[0].set(omega_hi).at[1].set(omega_mid).at[2].set(omega_lo)
    chunks = right_factor.reshape(k_block, n_freq, j_cols).transpose(1, 0, 2)
    chunks = jnp.concatenate(
        [chunks, jnp.broadcast_to(terms[None, :, None], (n_freq, 8, j_cols))], axis=1)
    chunks = lax.all_to_all(chunks, "freq", 0, 0, tiled=True)
    parts = chunks[:, k_block:k_block + 3, 0].astype(jnp.float32)
    omegas = (parts[:, 0] + parts[:, 1]) + parts[:, 2]
    right_cols = chunks[:, :k_block].reshape(n_freq * k_block, j_cols)
    observed = lax.all_to_all(measured, "freq", 3, 1, tiled=True)
    left_whole = lax.all_gather(left_factor, "freq", axis=1, tiled=True)
    total_samples = omegas.shape[0]
    grad_scale = float(RANKS) ** 0.25 / math.sqrt(float(total_samples * PORTS))
    left_wide = left_whole.astype(jnp.float32)
    right_wide = right_cols.astype(jnp.float32)
    denominator = pole_rates[None, :] * pole_rates[None, :] + omegas[:, None] * omegas[:, None]
    real_resp = jnp.repeat(pole_rates[None, :] / denominator, RANK, axis=1)
    imag_resp = jnp.repeat(-omegas[:, None] / denominator, RANK, axis=1)
    resp = jnp.stack([real_resp, imag_resp], 0)
    scaled_right = resp[:, :, :, None] * right_wide[None, None]
    fitted = jnp.einsum("rk,pfkj->pfrj", left_wide, scaled_right, precision=highest,
                        preferred_element_type=jnp.float32)
    fitted = lax.optimization_barrier(fitted)
    misfit = fitted - observed
    grad_left = jnp.einsum("pfrj,pfkj->rk", misfit, scaled_right, precision=highest,
                           preferred_element_type=jnp.float32)
    grad_left = lax.psum_scatter(grad_left * grad_scale, "freq", scatter_dimension=1, tiled=True)
    grad_left = lax.psum_scatter(grad_left, "inp", scatter_dimension=1, tiled=True)
    scaled_left = resp[:, :, None, :] * left_wide[None, None]
    grad_right = jnp.einsum("pfrk,pfrj->kj", scaled_left, misfit, precision=highest,
                            preferred_element_type=jnp.float32)
    k_rows, j_cols = grad_right.shape
    block = k_rows // (n_freq * n_outp)
    grad_right = (grad_right * grad_scale).reshape(n_freq, n_outp, block, j_cols)
    grad_right = grad_right.reshape(n_freq * n_outp, block, j_cols)
    grad_right = lax.all_to_all(grad_right, ("freq", "outp"), 0, 0, tiled=True)
    grad_right = jnp.sum(grad_right.reshape(n_freq, n_outp, block, j_cols), axis=1)
    grad_right = grad_right.transpose(1, 0, 2).reshape(block, n_freq * j_cols)
    return (grad_left, grad_right)


def solution(mesh):
    return jax.shard_map(
        shards,
        mesh=mesh,
        in_specs=(
            P(None, "freq", "outp", "inp"),
            P("outp", "freq"),
            P("freq", "inp"),
            P(),
            P("freq"),
        ),
        out_specs=(P("outp", ("freq", "inp")), P(("freq", "outp"), "inp")),
        check_vma=False,
    )
```

```python
import math

import jax
import jax.numpy as jnp
from jax import lax
from jax.sharding import PartitionSpec as P


PORTS = 2048
RANK = 8
RANKS = 4096


def shards(measured, left_factor, right_factor, pole_rates, sample_freqs):
    highest = lax.Precision.HIGH
    n_freq = lax.axis_size("freq")
    n_outp = lax.axis_size("outp")
    _, _, _, in_cols = measured.shape
    k_block = right_factor.shape[0]
    j_cols = in_cols // n_freq
    omega = sample_freqs[0]
    omega_hi = omega.astype(jnp.bfloat16)
    rest = omega - omega_hi.astype(jnp.float32)
    omega_mid = rest.astype(jnp.bfloat16)
    omega_lo = (rest - omega_mid.astype(jnp.float32)).astype(jnp.bfloat16)
    terms = jnp.zeros((8,), jnp.bfloat16).at[0].set(omega_hi).at[1].set(omega_mid).at[2].set(omega_lo)
    chunks = right_factor.reshape(k_block, n_freq, j_cols).transpose(1, 0, 2)
    chunks = jnp.concatenate(
        [chunks, jnp.broadcast_to(terms[None, :, None], (n_freq, 8, j_cols))], axis=1)
    chunks = lax.all_to_all(chunks, "freq", 0, 0, tiled=True)
    parts = chunks[:, k_block:k_block + 3, 0].astype(jnp.float32)
    omegas = (parts[:, 0] + parts[:, 1]) + parts[:, 2]
    right_cols = chunks[:, :k_block].reshape(n_freq * k_block, j_cols)
    observed = lax.all_to_all(measured, "freq", 3, 1, tiled=True)
    left_whole = lax.all_gather(left_factor, "freq", axis=1, tiled=True)
    total_samples = omegas.shape[0]
    grad_scale = float(RANKS) ** 0.25 / math.sqrt(float(total_samples * PORTS))
    left_wide = left_whole.astype(jnp.float32)
    right_wide = right_cols.astype(jnp.float32)
    denominator = pole_rates[None, :] * pole_rates[None, :] + omegas[:, None] * omegas[:, None]
    real_resp = jnp.repeat(pole_rates[None, :] / denominator, RANK, axis=1)
    imag_resp = jnp.repeat(-omegas[:, None] / denominator, RANK, axis=1)
    resp = jnp.stack([real_resp, imag_resp], 0)
    scaled_right = resp[:, :, :, None] * right_wide[None, None]
    fitted = jnp.einsum("rk,pfkj->pfrj", left_wide, scaled_right, precision=highest,
                        preferred_element_type=jnp.float32)
    fitted = lax.optimization_barrier(fitted)
    misfit = fitted - observed
    grad_left = jnp.einsum("pfrj,pfkj->rk", misfit, scaled_right, precision=highest,
                           preferred_element_type=jnp.float32)
    grad_left = lax.psum_scatter(grad_left * grad_scale, "freq", scatter_dimension=1, tiled=True)
    pair = grad_left.reshape(grad_left.shape[0], 2, grad_left.shape[1] // 2)
    side = lax.axis_index("inp")
    mine = lax.dynamic_index_in_dim(pair, side, 1, keepdims=False)
    theirs = lax.dynamic_index_in_dim(pair, 1 - side, 1, keepdims=False)
    grad_left = mine + lax.ppermute(theirs, "inp", [(0, 1), (1, 0)])
    scaled_left = resp[:, :, None, :] * left_wide[None, None]
    grad_right = jnp.einsum("pfrk,pfrj->kj", scaled_left, misfit, precision=highest,
                            preferred_element_type=jnp.float32)
    k_rows, j_cols = grad_right.shape
    block = k_rows // (n_freq * n_outp)
    grad_right = (grad_right * grad_scale).reshape(n_freq, n_outp, block, j_cols)
    grad_right = grad_right.reshape(n_freq * n_outp, block, j_cols)
    grad_right = lax.all_to_all(grad_right, ("freq", "outp"), 0, 0, tiled=True)
    grad_right = jnp.sum(grad_right.reshape(n_freq, n_outp, block, j_cols), axis=1)
    grad_right = grad_right.transpose(1, 0, 2).reshape(block, n_freq * j_cols)
    return (grad_left, grad_right)


def solution(mesh):
    return jax.shard_map(
        shards,
        mesh=mesh,
        in_specs=(
            P(None, "freq", "outp", "inp"),
            P("outp", "freq"),
            P("freq", "inp"),
            P(),
            P("freq"),
        ),
        out_specs=(P("outp", ("freq", "inp")), P(("freq", "outp"), "inp")),
        check_vma=False,
    )
```
